32 devices in a mesh: sta: 2 (over y), evt: 2 (over core), mode: 8 (over z, x).
Axes of the slice: x: 2, y: 2, z: 4, core: 2. Of those that a mesh axis runs over, the one named last changes fastest.
Arguments:
- receivers: bfloat16 [768, 32768], P('sta', ('mode', 'evt')), may hold values from -6 to 6
- excitations: bfloat16 [32768, 512], P(('mode', 'sta'), 'evt'), may hold values from -0.00390625 to 0.00390625
- mode_freqs: float32 [32768], P('mode'), may hold values from 0 to 1
- mode_damping: float32 [32768], P('mode'), may hold values from 0.02 to 0.2
- sample_freqs: float32 [8], replicated, may hold values from 0.2 to 0.8
Outputs:
- spectra: float32 [768, 2, 8, 512], P(('sta', 'mode'), None, None, 'evt')
The draws below stay inside these ranges and needn't reach their ends.
All inputs are finite; a program needn't handle non-finite values.
Results may differ from the reference program's by a relative error of at most 0.0029.
Values may be sent and summed in bfloat16 or wider, within the bound.
No kernel may reach another device: no remote copies, remote signals or barrier semaphores. Data moves between devices by JAX's collectives and lax.ppermute only.
A program may use at most 128 MiB of HBM per device.

```python
import math
import jax
import jax.numpy as jnp
from jax import lax

MODES = 32768
NF = 8
ROWS = 768
EVENTS = 512


def with_spikes(result, key, source, target, parts, factor):
    owner, partner = [(jnp.arange(result.shape[position]) // (result.shape[position] // parts)).reshape([-1 if axis == position else 1 for axis in range(result.ndim)]) for position in (source, target)]
    chosen = jax.random.permutation(key, parts)[partner]
    strong = (owner == chosen) | (owner == (partner + parts // 2) % parts)
    return jnp.where(strong, factor * result, result)


def steps_of(stream_key, dims, shards, low, high):
    gain = 1.0
    for axis_at, parts in shards:
        steps = jax.random.uniform(jax.random.fold_in(jax.random.fold_in(stream_key, 6), axis_at), (parts,), jnp.float32, low / len(shards), high / len(shards))
        gain = gain * jnp.repeat(jnp.exp(steps), dims[axis_at] // parts).reshape((-1,) + (1,) * (len(dims) - 1 - axis_at))
    return gain


def bell_draw(stream_key, extent, spread, limit, split=(), held_as=jnp.bfloat16):
    array = spread * jax.random.normal(stream_key, extent, jnp.float32)
    if split:
        array = array * steps_of(stream_key, extent, split, -0.22, 0.18)
    return jnp.clip(array, -limit, limit).astype(held_as)


def heavy_noise(own_key, extent, scale, reach, split, heavy, held_as=jnp.bfloat16):
    array = scale * jax.random.normal(own_key, extent, jnp.float32)
    if split:
        array = array * steps_of(own_key, extent, split, -0.22, 0.18)
    return jnp.clip(with_spikes(array, jax.random.fold_in(own_key, 3), *heavy), -reach, reach).astype(held_as)


def setup_inputs(seed: int = 0) -> dict:
    keys = jax.random.split(jax.random.key(seed), 6)
    receivers = heavy_noise(keys[0], (ROWS, MODES), 1.0, 6.0, ((0, 2), (1, 16)), (1, 0, 16, 2.0))
    excitations = bell_draw(keys[1], (MODES, EVENTS), (64 * MODES) ** -0.5, 0.00390625, ((0, 16), (1, 2)))
    mode_freqs = jnp.clip(1.0 * jax.random.uniform(keys[2], (MODES,), jnp.float32) ** steps_of(keys[2], (MODES,), ((0, 8),), -0.2, 0.2), 0.0, 1.0)
    mode_damping = jnp.clip(jnp.exp(math.log(0.2) - 2.3025851 * jax.random.uniform(keys[3], (MODES,), jnp.float32) ** steps_of(keys[3], (MODES,), ((0, 8),), -0.2, 0.2)), 0.02, 0.2)
    sample_freqs = jnp.clip(jax.random.uniform(keys[4], (NF,), jnp.float32, 0.2, 0.8), 0.2, 0.8)
    return dict(receivers=receivers, excitations=excitations, mode_freqs=mode_freqs, mode_damping=mode_damping, sample_freqs=sample_freqs)


def resonance(mode_freqs, mode_damping, frequency):
    offset = mode_freqs - frequency
    denominator = offset * offset + mode_damping * mode_damping
    return mode_damping / denominator, -offset / denominator


def reference(receivers, excitations, mode_freqs, mode_damping, sample_freqs):
    def per_frequency(frequency):
        real_weight, imag_weight = resonance(mode_freqs, mode_damping, frequency)
        widened = receivers.astype(jnp.float32)
        weighted = jnp.stack([widened * real_weight, widened * imag_weight], axis=1).astype(jnp.bfloat16)
        product = jnp.dot(weighted.reshape(2 * ROWS, MODES), excitations, preferred_element_type=jnp.float32)
        return product.reshape(ROWS, 2, EVENTS)

    spectra = lax.map(per_frequency, sample_freqs)
    return jnp.transpose(spectra, (1, 2, 0, 3))
```

```python
import jax
import jax.numpy as jnp
from jax import lax
from jax.sharding import PartitionSpec as P


def resonance(mode_freqs, mode_damping, frequency):
    offset = mode_freqs - frequency
    denominator = offset * offset + mode_damping * mode_damping
    return (mode_damping / denominator, -offset / denominator)


def per_device(receivers, excitations, mode_freqs, mode_damping, sample_freqs):
    receiver_block = lax.all_gather(receivers, "evt", axis=1, tiled=True)
    source_block = lax.all_gather(excitations, "sta", axis=0, tiled=True)
    row_count, mode_count = receiver_block.shape
    real_weight, imag_weight = resonance(
        mode_freqs[None, :], mode_damping[None, :], sample_freqs[:, None]
    )
    weights = jnp.stack([real_weight, imag_weight], axis=0)
    widened = receiver_block.astype(jnp.float32)
    weighted = (widened[:, None, None, :] * weights[None]).astype(jnp.bfloat16)
    partial = jnp.dot(
        weighted.reshape(-1, mode_count), source_block, preferred_element_type=jnp.float32
    )
    partial = partial.reshape(row_count, 2, sample_freqs.shape[0], source_block.shape[1])
    return lax.psum_scatter(partial, "mode", scatter_dimension=0, tiled=True)


def solution(mesh):
    placed = (P("sta", ("mode", "evt")), P(("mode", "sta"), "evt"), P("mode"), P("mode"), P())
    return jax.shard_map(
        per_device,
        mesh=mesh,
        in_specs=placed,
        out_specs=P(("sta", "mode"), None, None, "evt"),
        check_vma=False,
    )
```

```python
import jax
import jax.numpy as jnp
from jax import lax
from jax.sharding import PartitionSpec as P


def resonance(mode_freqs, mode_damping, frequency):
    offset = mode_freqs - frequency
    denominator = offset * offset + mode_damping * mode_damping
    return (mode_damping / denominator, -offset / denominator)


def ring_order(count):
    if count % 2:
        return list(range(count))
    return [2 * i for i in range(count // 2)] + [2 * i + 1 for i in reversed(range(count // 2))]


def swap_pair(local, axis_name):
    return lax.ppermute(local, axis_name, [(0, 1), (1, 0)])


def gather_blocks(local, axis_name, size, axis):
    if size != 2:
        return lax.all_gather(local, axis_name, axis=axis, tiled=True)
    other = swap_pair(local, axis_name)
    index = lax.axis_index(axis_name)
    first = jnp.where(index == 0, local, other)
    second = jnp.where(index == 0, other, local)
    return jnp.concatenate([first, second], axis=axis)


def make_per_device(sizes):
    mode_count = sizes["mode"]
    order = ring_order(mode_count)
    position_of = [0] * mode_count
    for position, device in enumerate(order):
        position_of[device] = position
    clockwise = [(order[i], order[(i + 1) % mode_count]) for i in range(mode_count)]
    counter = [(order[(i + 1) % mode_count], order[i]) for i in range(mode_count)]

    def per_device(receivers, excitations, mode_freqs, mode_damping, sample_freqs):
        mode = lax.axis_index("mode")
        receiver_block = gather_blocks(receivers, "evt", sizes["evt"], 1)
        source_block = gather_blocks(excitations, "sta", sizes["sta"], 0)
        row_count, block_modes = receiver_block.shape
        real_weight, imag_weight = resonance(
            mode_freqs[None, :], mode_damping[None, :], sample_freqs[:, None]
        )
        weights = jnp.stack([real_weight, imag_weight], axis=0)
        chunk = row_count // mode_count
        half = chunk // 2
        order_table = jnp.asarray(order, dtype=jnp.int32)
        position = jnp.asarray(position_of, dtype=jnp.int32)[mode]

        def partial_rows(owner, part):
            start = owner * chunk + part * half
            rows = lax.dynamic_slice_in_dim(receiver_block, start, half, axis=0)
            widened = rows.astype(jnp.float32)
            weighted = (widened[:, None, None, :] * weights[None]).astype(jnp.bfloat16)
            product = jnp.dot(
                weighted.reshape(-1, block_modes), source_block, preferred_element_type=jnp.float32
            )
            return product.reshape(half, 2, sample_freqs.shape[0], source_block.shape[1])

        def owner_at(offset):
            return order_table[(position + offset) % mode_count]

        ahead = partial_rows(owner_at(-1), 0)
        behind = partial_rows(owner_at(1), 1)
        for step in range(mode_count - 1):
            ahead = lax.ppermute(ahead, "mode", clockwise)
            behind = lax.ppermute(behind, "mode", counter)
            ahead = ahead + partial_rows(owner_at(-step - 2), 0)
            behind = behind + partial_rows(owner_at(step + 2), 1)
        return jnp.concatenate([ahead, behind], axis=0)

    return per_device


def solution(mesh):
    placed = (P("sta", ("mode", "evt")), P(("mode", "sta"), "evt"), P("mode"), P("mode"), P())
    return jax.shard_map(
        make_per_device(dict(mesh.shape)),
        mesh=mesh,
        in_specs=placed,
        out_specs=P(("sta", "mode"), None, None, "evt"),
        check_vma=False,
    )
```

```python
import jax
import jax.numpy as jnp
from jax import lax
from jax.sharding import PartitionSpec as P


def resonance(mode_freqs, mode_damping, frequency):
    offset = mode_freqs - frequency
    denominator = offset * offset + mode_damping * mode_damping
    return (mode_damping / denominator, -offset / denominator)


def ring_order(count):
    if count % 2:
        return list(range(count))
    return [2 * i for i in range(count // 2)] + [2 * i + 1 for i in reversed(range(count // 2))]


def swap_pair(local, axis_name):
    return lax.ppermute(local, axis_name, [(0, 1), (1, 0)])


def gather_blocks(local, axis_name, size, axis):
    if size != 2:
        return lax.all_gather(local, axis_name, axis=axis, tiled=True)
    other = swap_pair(local, axis_name)
    index = lax.axis_index(axis_name)
    first = jnp.where(index == 0, local, other)
    second = jnp.where(index == 0, other, local)
    return jnp.concatenate([first, second], axis=axis)


def make_per_device(sizes):
    mode_count = sizes["mode"]
    order = ring_order(mode_count)
    position_of = [0] * mode_count
    for position, device in enumerate(order):
        position_of[device] = position
    clockwise = [(order[i], order[(i + 1) % mode_count]) for i in range(mode_count)]
    counter = [(order[(i + 1) % mode_count], order[i]) for i in range(mode_count)]

    def per_device(receivers, excitations, mode_freqs, mode_damping, sample_freqs):
        mode = lax.axis_index("mode")
        receiver_block = gather_blocks(receivers, "evt", sizes["evt"], 1)
        pieces = 2
        width = excitations.shape[1] // pieces
        source_blocks = [
            gather_blocks(excitations[:, q * width : (q + 1) * width], "sta", sizes["sta"], 0)
            for q in range(pieces)
        ]
        row_count, block_modes = receiver_block.shape
        real_weight, imag_weight = resonance(
            mode_freqs[None, :], mode_damping[None, :], sample_freqs[:, None]
        )
        weights = jnp.stack([real_weight, imag_weight], axis=0)
        chunk = row_count // mode_count
        half = chunk // 2
        order_table = jnp.asarray(order, dtype=jnp.int32)
        position = jnp.asarray(position_of, dtype=jnp.int32)[mode]

        def partial_rows(owner, part, source_block):
            start = owner * chunk + part * half
            rows = lax.dynamic_slice_in_dim(receiver_block, start, half, axis=0)
            widened = rows.astype(jnp.float32)
            weighted = (widened[:, None, None, :] * weights[None]).astype(jnp.bfloat16)
            product = jnp.dot(
                weighted.reshape(-1, block_modes), source_block, preferred_element_type=jnp.float32
            )
            return product.reshape(half, 2, sample_freqs.shape[0], source_block.shape[1])

        def owner_at(offset):
            return order_table[(position + offset) % mode_count]

        ahead = [partial_rows(owner_at(-1), 0, source) for source in source_blocks]
        behind = [partial_rows(owner_at(1), 1, source) for source in source_blocks]
        for step in range(mode_count - 1):
            for q, source in enumerate(source_blocks):
                ahead[q] = lax.ppermute(ahead[q], "mode", clockwise)
                behind[q] = lax.ppermute(behind[q], "mode", counter)
                ahead[q] = ahead[q] + partial_rows(owner_at(-step - 2), 0, source)
                behind[q] = behind[q] + partial_rows(owner_at(step + 2), 1, source)
        rows = [jnp.concatenate(parts, axis=3) for parts in (ahead, behind)]
        return jnp.concatenate(rows, axis=0)

    return per_device


def solution(mesh):
    placed = (P("sta", ("mode", "evt")), P(("mode", "sta"), "evt"), P("mode"), P("mode"), P())
    return jax.shard_map(
        make_per_device(dict(mesh.shape)),
        mesh=mesh,
        in_specs=placed,
        out_specs=P(("sta", "mode"), None, None, "evt"),
        check_vma=False,
    )
```

```python
import jax
import jax.numpy as jnp
from jax import lax
from jax.sharding import PartitionSpec as P


def resonance(mode_freqs, mode_damping, frequency):
    offset = mode_freqs - frequency
    denominator = offset * offset + mode_damping * mode_damping
    return (mode_damping / denominator, -offset / denominator)


def ring_order(count):
    if count % 2:
        return list(range(count))
    return [2 * i for i in range(count // 2)] + [2 * i + 1 for i in reversed(range(count // 2))]


def swap_pair(local, axis_name):
    return lax.ppermute(local, axis_name, [(0, 1), (1, 0)])


def gather_blocks(local, axis_name, size, axis):
    if size != 2:
        return lax.all_gather(local, axis_name, axis=axis, tiled=True)
    other = swap_pair(local, axis_name)
    index = lax.axis_index(axis_name)
    first = jnp.where(index == 0, local, other)
    second = jnp.where(index == 0, other, local)
    return jnp.concatenate([first, second], axis=axis)


def make_per_device(sizes):
    mode_count = sizes["mode"]
    order = ring_order(mode_count)
    position_of = [0] * mode_count
    for position, device in enumerate(order):
        position_of[device] = position
    clockwise = [(order[i], order[(i + 1) % mode_count]) for i in range(mode_count)]
    counter = [(order[(i + 1) % mode_count], order[i]) for i in range(mode_count)]

    def per_device(receivers, excitations, mode_freqs, mode_damping, sample_freqs):
        mode = lax.axis_index("mode")
        receiver_block = gather_blocks(receivers, "evt", sizes["evt"], 1)
        pieces = 2
        width = excitations.shape[1] // pieces
        source_blocks = [
            gather_blocks(excitations[:, q * width : (q + 1) * width], "sta", sizes["sta"], 0)
            for q in range(pieces)
        ]
        row_count, block_modes = receiver_block.shape
        real_weight, imag_weight = resonance(
            mode_freqs[None, :], mode_damping[None, :], sample_freqs[:, None]
        )
        weights = jnp.stack([real_weight, imag_weight], axis=0)
        chunk = row_count // mode_count
        half = chunk // 2
        order_table = jnp.asarray(order, dtype=jnp.int32)
        position = jnp.asarray(position_of, dtype=jnp.int32)[mode]

        def partial_rows(owner, part, source_block, receiver_block=receiver_block):
            start = owner * chunk + part * half
            rows = lax.dynamic_slice_in_dim(receiver_block, start, half, axis=0)
            widened = rows.astype(jnp.float32)
            weighted = (widened[:, None, None, :] * weights[None]).astype(jnp.bfloat16)
            product = jnp.dot(
                weighted.reshape(-1, block_modes), source_block, preferred_element_type=jnp.float32
            )
            return product.reshape(half, 2, sample_freqs.shape[0], source_block.shape[1])

        def owner_at(offset):
            return order_table[(position + offset) % mode_count]

        ahead = [partial_rows(owner_at(-1), 0, source) for source in source_blocks]
        behind = [partial_rows(owner_at(1), 1, source) for source in source_blocks]
        for step in range(mode_count - 1):
            for q, source in enumerate(source_blocks):
                held, gated, sent_ahead, sent_behind = lax.optimization_barrier(
                    (receiver_block, source, ahead[q], behind[q])
                )
                ahead[q] = lax.ppermute(sent_ahead, "mode", clockwise)
                behind[q] = lax.ppermute(sent_behind, "mode", counter)
                ahead[q] = ahead[q] + partial_rows(owner_at(-step - 2), 0, gated, held)
                behind[q] = behind[q] + partial_rows(owner_at(step + 2), 1, gated, held)
        rows = [jnp.concatenate(parts, axis=3) for parts in (ahead, behind)]
        return jnp.concatenate(rows, axis=0)

    return per_device


def solution(mesh):
    placed = (P("sta", ("mode", "evt")), P(("mode", "sta"), "evt"), P("mode"), P("mode"), P())
    return jax.shard_map(
        make_per_device(dict(mesh.shape)),
        mesh=mesh,
        in_specs=placed,
        out_specs=P(("sta", "mode"), None, None, "evt"),
        check_vma=False,
    )
```

```python
import jax
import jax.numpy as jnp
from jax import lax
from jax.sharding import PartitionSpec as P


def resonance(mode_freqs, mode_damping, frequency):
    offset = mode_freqs - frequency
    denominator = offset * offset + mode_damping * mode_damping
    return (mode_damping / denominator, -offset / denominator)


def ring_order(count):
    if count % 2:
        return list(range(count))
    return [2 * i for i in range(count // 2)] + [2 * i + 1 for i in reversed(range(count // 2))]


def swap_pair(local, axis_name):
    return lax.ppermute(local, axis_name, [(0, 1), (1, 0)])


def gather_blocks(local, axis_name, size, axis):
    if size != 2:
        return lax.all_gather(local, axis_name, axis=axis, tiled=True)
    other = swap_pair(local, axis_name)
    index = lax.axis_index(axis_name)
    first = jnp.where(index == 0, local, other)
    second = jnp.where(index == 0, other, local)
    return jnp.concatenate([first, second], axis=axis)


def make_per_device(sizes):
    mode_count = sizes["mode"]
    order = ring_order(mode_count)
    position_of = [0] * mode_count
    for position, device in enumerate(order):
        position_of[device] = position
    clockwise = [(order[i], order[(i + 1) % mode_count]) for i in range(mode_count)]
    counter = [(order[(i + 1) % mode_count], order[i]) for i in range(mode_count)]

    def per_device(receivers, excitations, mode_freqs, mode_damping, sample_freqs):
        mode = lax.axis_index("mode")
        receiver_block = lax.all_gather(receivers, "evt", axis=1, tiled=True)
        source_block = gather_blocks(excitations, "sta", sizes["sta"], 0)
        row_count, block_modes = receiver_block.shape
        real_weight, imag_weight = resonance(
            mode_freqs[None, :], mode_damping[None, :], sample_freqs[:, None]
        )
        weights = jnp.stack([real_weight, imag_weight], axis=0)
        chunk = row_count // mode_count
        half = chunk // 2
        order_table = jnp.asarray(order, dtype=jnp.int32)
        position = jnp.asarray(position_of, dtype=jnp.int32)[mode]

        def partial_rows(owner, part):
            start = owner * chunk + part * half
            rows = lax.dynamic_slice_in_dim(receiver_block, start, half, axis=0)
            widened = rows.astype(jnp.float32)
            weighted = (widened[:, None, None, :] * weights[None]).astype(jnp.bfloat16)
            product = jnp.dot(
                weighted.reshape(-1, block_modes), source_block, preferred_element_type=jnp.float32
            )
            return product.reshape(half, 2, sample_freqs.shape[0], source_block.shape[1])

        def owner_at(offset):
            return order_table[(position + offset) % mode_count]

        ahead = partial_rows(owner_at(-1), 0)
        behind = partial_rows(owner_at(1), 1)
        for step in range(mode_count - 1):
            ahead = lax.ppermute(ahead, "mode", clockwise)
            behind = lax.ppermute(behind, "mode", counter)
            ahead = ahead + partial_rows(owner_at(-step - 2), 0)
            behind = behind + partial_rows(owner_at(step + 2), 1)
        return jnp.concatenate([ahead, behind], axis=0)

    return per_device


def solution(mesh):
    placed = (P("sta", ("mode", "evt")), P(("mode", "sta"), "evt"), P("mode"), P("mode"), P())
    return jax.shard_map(
        make_per_device(dict(mesh.shape)),
        mesh=mesh,
        in_specs=placed,
        out_specs=P(("sta", "mode"), None, None, "evt"),
        check_vma=False,
    )
```

```python
import jax
import jax.numpy as jnp
from jax import lax
from jax.sharding import PartitionSpec as P


def resonance(mode_freqs, mode_damping, frequency):
    offset = mode_freqs - frequency
    denominator = offset * offset + mode_damping * mode_damping
    return (mode_damping / denominator, -offset / denominator)


def ring_order(count):
    if count % 2:
        return list(range(count))
    return [2 * i for i in range(count // 2)] + [2 * i + 1 for i in reversed(range(count // 2))]


def swap_pair(local, axis_name):
    return lax.ppermute(local, axis_name, [(0, 1), (1, 0)])


def gather_blocks(local, axis_name, size, axis):
    if size != 2:
        return lax.all_gather(local, axis_name, axis=axis, tiled=True)
    other = swap_pair(local, axis_name)
    index = lax.axis_index(axis_name)
    first = jnp.where(index == 0, local, other)
    second = jnp.where(index == 0, other, local)
    return jnp.concatenate([first, second], axis=axis)


def make_per_device(sizes):
    mode_count = sizes["mode"]
    order = ring_order(mode_count)
    position_of = [0] * mode_count
    for position, device in enumerate(order):
        position_of[device] = position
    clockwise = [(order[i], order[(i + 1) % mode_count]) for i in range(mode_count)]
    counter = [(order[(i + 1) % mode_count], order[i]) for i in range(mode_count)]

    def per_device(receivers, excitations, mode_freqs, mode_damping, sample_freqs):
        mode = lax.axis_index("mode")
        receiver_block = gather_blocks(receivers, "evt", sizes["evt"], 1)
        width = excitations.shape[1] // 2
        first_source = gather_blocks(excitations[:, :width], "sta", sizes["sta"], 0)
        second_local, _ = lax.optimization_barrier((excitations[:, width:], first_source))
        if sizes["sta"] == 2:
            second_far = swap_pair(second_local, "sta")
        else:
            second_far = lax.all_gather(second_local, "sta", axis=0, tiled=True)
        row_count, block_modes = receiver_block.shape
        real_weight, imag_weight = resonance(
            mode_freqs[None, :], mode_damping[None, :], sample_freqs[:, None]
        )
        weights = jnp.stack([real_weight, imag_weight], axis=0)
        chunk = row_count // mode_count
        half = chunk // 2
        order_table = jnp.asarray(order, dtype=jnp.int32)
        position = jnp.asarray(position_of, dtype=jnp.int32)[mode]

        def partial_rows(owner, part, source_block, receiver_block=receiver_block):
            start = owner * chunk + part * half
            rows = lax.dynamic_slice_in_dim(receiver_block, start, half, axis=0)
            widened = rows.astype(jnp.float32)
            weighted = (widened[:, None, None, :] * weights[None]).astype(jnp.bfloat16)
            product = jnp.dot(
                weighted.reshape(-1, block_modes), source_block, preferred_element_type=jnp.float32
            )
            return product.reshape(half, 2, sample_freqs.shape[0], source_block.shape[1])

        def owner_at(offset):
            return order_table[(position + offset) % mode_count]

        def start(source, held=receiver_block):
            return (
                partial_rows(owner_at(-1), 0, source, held),
                partial_rows(owner_at(1), 1, source, held),
            )

        def ring_step(step, sums, source):
            held, gated, sent_ahead, sent_behind = lax.optimization_barrier(
                (receiver_block, source, sums[0], sums[1])
            )
            ahead = lax.ppermute(sent_ahead, "mode", clockwise)
            behind = lax.ppermute(sent_behind, "mode", counter)
            return (
                ahead + partial_rows(owner_at(-step - 2), 0, gated, held),
                behind + partial_rows(owner_at(step + 2), 1, gated, held),
            )

        steps = mode_count - 1
        first = ring_step(0, start(first_source), first_source)
        held, second_far, _, _ = lax.optimization_barrier(
            (receiver_block, second_far, first[0], first[1])
        )
        if sizes["sta"] == 2:
            index = lax.axis_index("sta")
            second_source = jnp.concatenate(
                [
                    jnp.where(index == 0, second_local, second_far),
                    jnp.where(index == 0, second_far, second_local),
                ],
                axis=0,
            )
        else:
            second_source = second_far
        second = start(second_source, held)
        for step in range(1, steps):
            first = ring_step(step, first, first_source)
            second = ring_step(step - 1, second, second_source)
        second = ring_step(steps - 1, second, second_source)
        rows = [jnp.concatenate(parts, axis=3) for parts in zip(first, second)]
        return jnp.concatenate(rows, axis=0)

    return per_device


def solution(mesh):
    placed = (P("sta", ("mode", "evt")), P(("mode", "sta"), "evt"), P("mode"), P("mode"), P())
    return jax.shard_map(
        make_per_device(dict(mesh.shape)),
        mesh=mesh,
        in_specs=placed,
        out_specs=P(("sta", "mode"), None, None, "evt"),
        check_vma=False,
    )
```

```python
import jax
import jax.numpy as jnp
from jax import lax
from jax.sharding import PartitionSpec as P


def resonance(mode_freqs, mode_damping, frequency):
    offset = mode_freqs - frequency
    denominator = offset * offset + mode_damping * mode_damping
    return (mode_damping / denominator, -offset / denominator)


def ring_order(count):
    if count % 2:
        return list(range(count))
    return [2 * i for i in range(count // 2)] + [2 * i + 1 for i in reversed(range(count // 2))]


def swap_pair(local, axis_name):
    return lax.ppermute(local, axis_name, [(0, 1), (1, 0)])


def gather_blocks(local, axis_name, size, axis):
    if size != 2:
        return lax.all_gather(local, axis_name, axis=axis, tiled=True)
    other = swap_pair(local, axis_name)
    index = lax.axis_index(axis_name)
    first = jnp.where(index == 0, local, other)
    second = jnp.where(index == 0, other, local)
    return jnp.concatenate([first, second], axis=axis)


def make_per_device(sizes):
    mode_count = sizes["mode"]
    order = ring_order(mode_count)
    position_of = [0] * mode_count
    for position, device in enumerate(order):
        position_of[device] = position
    clockwise = [(order[i], order[(i + 1) % mode_count]) for i in range(mode_count)]
    counter = [(order[(i + 1) % mode_count], order[i]) for i in range(mode_count)]

    def per_device(receivers, excitations, mode_freqs, mode_damping, sample_freqs):
        mode = lax.axis_index("mode")
        receiver_block = gather_blocks(receivers, "evt", sizes["evt"], 1)
        source_block = gather_blocks(excitations, "sta", sizes["sta"], 0)
        row_count, block_modes = receiver_block.shape
        real_weight, imag_weight = resonance(
            mode_freqs[None, :], mode_damping[None, :], sample_freqs[:, None]
        )
        weights = jnp.stack([real_weight, imag_weight], axis=0)
        chunk = row_count // mode_count
        half = chunk // 3
        order_table = jnp.asarray(order, dtype=jnp.int32)
        position = jnp.asarray(position_of, dtype=jnp.int32)[mode]

        def partial_rows(owner, part):
            start = owner * chunk + part * half
            rows = lax.dynamic_slice_in_dim(receiver_block, start, half, axis=0)
            widened = rows.astype(jnp.float32)
            weighted = (widened[:, None, None, :] * weights[None]).astype(jnp.bfloat16)
            product = jnp.dot(
                weighted.reshape(-1, block_modes), source_block, preferred_element_type=jnp.float32
            )
            return product.reshape(half, 2, sample_freqs.shape[0], source_block.shape[1])

        def owner_at(offset):
            return order_table[(position + offset) % mode_count]

        offloaded_rows = receiver_block.reshape(mode_count, chunk, block_modes)[:, 2 * half :]
        widened = offloaded_rows.reshape(-1, block_modes).astype(jnp.float32)
        weighted = (widened[:, None, None, :] * weights[None]).astype(jnp.bfloat16)
        offloaded = jnp.dot(
            weighted.reshape(-1, block_modes), source_block, preferred_element_type=jnp.float32
        )
        offloaded = offloaded.reshape(-1, 2, sample_freqs.shape[0], source_block.shape[1])
        offloaded = lax.psum_scatter(offloaded, "mode", scatter_dimension=0, tiled=True)

        ahead = partial_rows(owner_at(-1), 0)
        behind = partial_rows(owner_at(1), 1)
        for step in range(mode_count - 1):
            ahead = lax.ppermute(ahead, "mode", clockwise)
            behind = lax.ppermute(behind, "mode", counter)
            ahead = ahead + partial_rows(owner_at(-step - 2), 0)
            behind = behind + partial_rows(owner_at(step + 2), 1)
        return jnp.concatenate([ahead, behind, offloaded], axis=0)

    return per_device


def solution(mesh):
    placed = (P("sta", ("mode", "evt")), P(("mode", "sta"), "evt"), P("mode"), P("mode"), P())
    return jax.shard_map(
        make_per_device(dict(mesh.shape)),
        mesh=mesh,
        in_specs=placed,
        out_specs=P(("sta", "mode"), None, None, "evt"),
        check_vma=False,
    )
```

```python
import jax
import jax.numpy as jnp
from jax import lax
from jax.sharding import PartitionSpec as P


def resonance(mode_freqs, mode_damping, frequency):
    offset = mode_freqs - frequency
    denominator = offset * offset + mode_damping * mode_damping
    return (mode_damping / denominator, -offset / denominator)


def ring_order(count):
    if count % 2:
        return list(range(count))
    return [2 * i for i in range(count // 2)] + [2 * i + 1 for i in reversed(range(count // 2))]


def swap_pair(local, axis_name):
    return lax.ppermute(local, axis_name, [(0, 1), (1, 0)])


def gather_blocks(local, axis_name, size, axis):
    if size != 2:
        return lax.all_gather(local, axis_name, axis=axis, tiled=True)
    other = swap_pair(local, axis_name)
    index = lax.axis_index(axis_name)
    first = jnp.where(index == 0, local, other)
    second = jnp.where(index == 0, other, local)
    return jnp.concatenate([first, second], axis=axis)


def make_per_device(sizes):
    mode_count = sizes["mode"]
    order = ring_order(mode_count)
    position_of = [0] * mode_count
    for position, device in enumerate(order):
        position_of[device] = position
    clockwise = [(order[i], order[(i + 1) % mode_count]) for i in range(mode_count)]
    counter = [(order[(i + 1) % mode_count], order[i]) for i in range(mode_count)]

    def per_device(receivers, excitations, mode_freqs, mode_damping, sample_freqs):
        mode = lax.axis_index("mode")
        receiver_block = gather_blocks(receivers, "evt", sizes["evt"], 1)
        width = excitations.shape[1] // 2
        first_source = gather_blocks(excitations[:, :width], "sta", sizes["sta"], 0)
        row_count, block_modes = receiver_block.shape
        real_weight, imag_weight = resonance(
            mode_freqs[None, :], mode_damping[None, :], sample_freqs[:, None]
        )
        weights = jnp.stack([real_weight, imag_weight], axis=0)
        chunk = row_count // mode_count
        half = chunk // 2
        order_table = jnp.asarray(order, dtype=jnp.int32)
        position = jnp.asarray(position_of, dtype=jnp.int32)[mode]

        def partial_rows(owner, part, source_block, receiver_block=receiver_block):
            start = owner * chunk + part * half
            rows = lax.dynamic_slice_in_dim(receiver_block, start, half, axis=0)
            widened = rows.astype(jnp.float32)
            weighted = (widened[:, None, None, :] * weights[None]).astype(jnp.bfloat16)
            product = jnp.dot(
                weighted.reshape(-1, block_modes), source_block, preferred_element_type=jnp.float32
            )
            return product.reshape(half, 2, sample_freqs.shape[0], source_block.shape[1])

        def owner_at(offset):
            return order_table[(position + offset) % mode_count]

        def start(source, held=receiver_block):
            return (
                partial_rows(owner_at(-1), 0, source, held),
                partial_rows(owner_at(1), 1, source, held),
            )

        def ring_step(step, sums, source):
            held, gated, sent_ahead, sent_behind = lax.optimization_barrier(
                (receiver_block, source, sums[0], sums[1])
            )
            ahead = lax.ppermute(sent_ahead, "mode", clockwise)
            behind = lax.ppermute(sent_behind, "mode", counter)
            return (
                ahead + partial_rows(owner_at(-step - 2), 0, gated, held),
                behind + partial_rows(owner_at(step + 2), 1, gated, held),
            )

        steps = mode_count - 1
        first = start(first_source)
        second_local, first_ahead, first_behind = lax.optimization_barrier(
            (excitations[:, width:], first[0], first[1])
        )
        if sizes["sta"] == 2:
            second_far = swap_pair(second_local, "sta")
        else:
            second_far = lax.all_gather(second_local, "sta", axis=0, tiled=True)
        first = ring_step(0, (first_ahead, first_behind), first_source)
        held, second_far, _, _ = lax.optimization_barrier(
            (receiver_block, second_far, first[0], first[1])
        )
        if sizes["sta"] == 2:
            index = lax.axis_index("sta")
            second_source = jnp.concatenate(
                [
                    jnp.where(index == 0, second_local, second_far),
                    jnp.where(index == 0, second_far, second_local),
                ],
                axis=0,
            )
        else:
            second_source = second_far
        second = start(second_source, held)
        for step in range(1, steps):
            first = ring_step(step, first, first_source)
            second = ring_step(step - 1, second, second_source)
        second = ring_step(steps - 1, second, second_source)
        rows = [jnp.concatenate(parts, axis=3) for parts in zip(first, second)]
        return jnp.concatenate(rows, axis=0)

    return per_device


def solution(mesh):
    placed = (P("sta", ("mode", "evt")), P(("mode", "sta"), "evt"), P("mode"), P("mode"), P())
    return jax.shard_map(
        make_per_device(dict(mesh.shape)),
        mesh=mesh,
        in_specs=placed,
        out_specs=P(("sta", "mode"), None, None, "evt"),
        check_vma=False,
    )
```

```python
import jax
import jax.numpy as jnp
from jax import lax
from jax.sharding import PartitionSpec as P


def resonance(mode_freqs, mode_damping, frequency):
    offset = mode_freqs - frequency
    denominator = offset * offset + mode_damping * mode_damping
    return (mode_damping / denominator, -offset / denominator)


def ring_order(count):
    if count % 2:
        return list(range(count))
    return [2 * i for i in range(count // 2)] + [2 * i + 1 for i in reversed(range(count // 2))]


def swap_pair(local, axis_name):
    return lax.ppermute(local, axis_name, [(0, 1), (1, 0)])


def gather_blocks(local, axis_name, size, axis):
    if size != 2:
        return lax.all_gather(local, axis_name, axis=axis, tiled=True)
    other = swap_pair(local, axis_name)
    index = lax.axis_index(axis_name)
    first = jnp.where(index == 0, local, other)
    second = jnp.where(index == 0, other, local)
    return jnp.concatenate([first, second], axis=axis)


def make_per_device(sizes):
    mode_count = sizes["mode"]
    order = ring_order(mode_count)
    position_of = [0] * mode_count
    for position, device in enumerate(order):
        position_of[device] = position
    clockwise = [(order[i], order[(i + 1) % mode_count]) for i in range(mode_count)]
    counter = [(order[(i + 1) % mode_count], order[i]) for i in range(mode_count)]

    def per_device(receivers, excitations, mode_freqs, mode_damping, sample_freqs):
        mode = lax.axis_index("mode")
        real_weight, imag_weight = resonance(
            mode_freqs[None, :], mode_damping[None, :], sample_freqs[:, None]
        )
        weights = jnp.stack([real_weight, imag_weight], axis=0)
        if mode_count % 2:
            position = mode
        else:
            position = jnp.where(mode % 2 == 0, mode // 2, mode_count - 1 - mode // 2)
        receivers, excitations, weights, position = lax.optimization_barrier(
            (receivers, excitations, weights, position)
        )
        receiver_block = gather_blocks(receivers, "evt", sizes["evt"], 1)
        width = excitations.shape[1] // 2
        first_source = gather_blocks(excitations[:, :width], "sta", sizes["sta"], 0)
        row_count, block_modes = receiver_block.shape
        chunk = row_count // mode_count
        half = chunk // 2

        def partial_rows(owner, part, source_block, receiver_block=receiver_block):
            start = owner * chunk + part * half
            rows = lax.dynamic_slice_in_dim(receiver_block, start, half, axis=0)
            widened = rows.astype(jnp.float32)
            weighted = (widened[:, None, None, :] * weights[None]).astype(jnp.bfloat16)
            product = jnp.dot(
                weighted.reshape(-1, block_modes), source_block, preferred_element_type=jnp.float32
            )
            return product.reshape(half, 2, sample_freqs.shape[0], source_block.shape[1])

        def owner_at(offset):
            place = (position + offset) % mode_count
            if mode_count % 2:
                return place
            return jnp.where(place < mode_count // 2, 2 * place, 2 * (mode_count - 1 - place) + 1)

        def start(source, held=receiver_block):
            return (
                partial_rows(owner_at(-1), 0, source, held),
                partial_rows(owner_at(1), 1, source, held),
            )

        def ring_step(step, sums, source):
            held, gated, sent_ahead, sent_behind = lax.optimization_barrier(
                (receiver_block, source, sums[0], sums[1])
            )
            ahead = lax.ppermute(sent_ahead, "mode", clockwise)
            behind = lax.ppermute(sent_behind, "mode", counter)
            return (
                ahead + partial_rows(owner_at(-step - 2), 0, gated, held),
                behind + partial_rows(owner_at(step + 2), 1, gated, held),
            )

        steps = mode_count - 1
        first = start(first_source)
        second_local, first_ahead, first_behind = lax.optimization_barrier(
            (excitations[:, width:], first[0], first[1])
        )
        if sizes["sta"] == 2:
            second_far = swap_pair(second_local, "sta")
        else:
            second_far = lax.all_gather(second_local, "sta", axis=0, tiled=True)
        first = ring_step(0, (first_ahead, first_behind), first_source)
        held, second_far, _, _ = lax.optimization_barrier(
            (receiver_block, second_far, first[0], first[1])
        )
        if sizes["sta"] == 2:
            index = lax.axis_index("sta")
            second_source = jnp.concatenate(
                [
                    jnp.where(index == 0, second_local, second_far),
                    jnp.where(index == 0, second_far, second_local),
                ],
                axis=0,
            )
        else:
            second_source = second_far
        second = start(second_source, held)
        for step in range(1, steps):
            first = ring_step(step, first, first_source)
            second = ring_step(step - 1, second, second_source)
        second = ring_step(steps - 1, second, second_source)
        rows = [jnp.concatenate(parts, axis=3) for parts in zip(first, second)]
        return jnp.concatenate(rows, axis=0)

    return per_device


def solution(mesh):
    placed = (P("sta", ("mode", "evt")), P(("mode", "sta"), "evt"), P("mode"), P("mode"), P())
    return jax.shard_map(
        make_per_device(dict(mesh.shape)),
        mesh=mesh,
        in_specs=placed,
        out_specs=P(("sta", "mode"), None, None, "evt"),
        check_vma=False,
    )
```

```python
import jax
import jax.numpy as jnp
from jax import lax
from jax.sharding import PartitionSpec as P


def resonance(mode_freqs, mode_damping, frequency):
    offset = mode_freqs - frequency
    denominator = offset * offset + mode_damping * mode_damping
    return (mode_damping / denominator, -offset / denominator)


def ring_order(count):
    if count % 2:
        return list(range(count))
    return [2 * i for i in range(count // 2)] + [2 * i + 1 for i in reversed(range(count // 2))]


def swap_pair(local, axis_name):
    return lax.ppermute(local, axis_name, [(0, 1), (1, 0)])


def gather_blocks(local, axis_name, size, axis):
    if size != 2:
        return lax.all_gather(local, axis_name, axis=axis, tiled=True)
    other = swap_pair(local, axis_name)
    index = lax.axis_index(axis_name)
    first = jnp.where(index == 0, local, other)
    second = jnp.where(index == 0, other, local)
    return jnp.concatenate([first, second], axis=axis)


def make_per_device(sizes):
    mode_count = sizes["mode"]
    order = ring_order(mode_count)
    position_of = [0] * mode_count
    for position, device in enumerate(order):
        position_of[device] = position
    clockwise = [(order[i], order[(i + 1) % mode_count]) for i in range(mode_count)]
    counter = [(order[(i + 1) % mode_count], order[i]) for i in range(mode_count)]

    def per_device(receivers, excitations, mode_freqs, mode_damping, sample_freqs):
        mode = lax.axis_index("mode")
        real_weight, imag_weight = resonance(
            mode_freqs[None, :], mode_damping[None, :], sample_freqs[:, None]
        )
        weights = jnp.stack([real_weight, imag_weight], axis=0)
        if mode_count % 2:
            position = mode
        else:
            position = jnp.where(mode % 2 == 0, mode // 2, mode_count - 1 - mode // 2)
        receivers, excitations, weights, position = lax.optimization_barrier(
            (receivers, excitations, weights, position)
        )
        receiver_block = gather_blocks(receivers, "evt", sizes["evt"], 1)
        source_block = gather_blocks(excitations, "sta", sizes["sta"], 0)
        row_count, block_modes = receiver_block.shape
        chunk = row_count // mode_count
        half = chunk // 2

        def partial_rows(owner, part):
            start = owner * chunk + part * half
            rows = lax.dynamic_slice_in_dim(receiver_block, start, half, axis=0)
            widened = rows.astype(jnp.float32)
            weighted = (widened[:, None, None, :] * weights[None]).astype(jnp.bfloat16)
            product = jnp.dot(
                weighted.reshape(-1, block_modes), source_block, preferred_element_type=jnp.float32
            )
            return product.reshape(half, 2, sample_freqs.shape[0], source_block.shape[1])

        def owner_at(offset):
            place = (position + offset) % mode_count
            if mode_count % 2:
                return place
            return jnp.where(place < mode_count // 2, 2 * place, 2 * (mode_count - 1 - place) + 1)

        ahead = partial_rows(owner_at(-1), 0)
        behind = partial_rows(owner_at(1), 1)
        for step in range(mode_count - 1):
            ahead = lax.ppermute(ahead, "mode", clockwise)
            behind = lax.ppermute(behind, "mode", counter)
            ahead = ahead + partial_rows(owner_at(-step - 2), 0)
            behind = behind + partial_rows(owner_at(step + 2), 1)
        return jnp.concatenate([ahead, behind], axis=0)

    return per_device


def solution(mesh):
    placed = (P("sta", ("mode", "evt")), P(("mode", "sta"), "evt"), P("mode"), P("mode"), P())
    return jax.shard_map(
        make_per_device(dict(mesh.shape)),
        mesh=mesh,
        in_specs=placed,
        out_specs=P(("sta", "mode"), None, None, "evt"),
        check_vma=False,
    )
```

```python
import jax
import jax.numpy as jnp
from jax import lax
from jax.sharding import PartitionSpec as P


def resonance(mode_freqs, mode_damping, frequency):
    offset = mode_freqs - frequency
    denominator = offset * offset + mode_damping * mode_damping
    return (mode_damping / denominator, -offset / denominator)


def ring_order(count):
    if count % 2:
        return list(range(count))
    return [2 * i for i in range(count // 2)] + [2 * i + 1 for i in reversed(range(count // 2))]


def swap_pair(local, axis_name):
    return lax.ppermute(local, axis_name, [(0, 1), (1, 0)])


def gather_blocks(local, axis_name, size, axis):
    if size != 2:
        return lax.all_gather(local, axis_name, axis=axis, tiled=True)
    other = swap_pair(local, axis_name)
    index = lax.axis_index(axis_name)
    first = jnp.where(index == 0, local, other)
    second = jnp.where(index == 0, other, local)
    return jnp.concatenate([first, second], axis=axis)


def make_per_device(sizes):
    mode_count = sizes["mode"]
    order = ring_order(mode_count)
    position_of = [0] * mode_count
    for position, device in enumerate(order):
        position_of[device] = position
    clockwise = [(order[i], order[(i + 1) % mode_count]) for i in range(mode_count)]
    counter = [(order[(i + 1) % mode_count], order[i]) for i in range(mode_count)]

    def per_device(receivers, excitations, mode_freqs, mode_damping, sample_freqs):
        mode = lax.axis_index("mode")
        real_weight, imag_weight = resonance(
            mode_freqs[None, :], mode_damping[None, :], sample_freqs[:, None]
        )
        weights = jnp.stack([real_weight, imag_weight], axis=0)
        if mode_count % 2:
            position = mode
        else:
            position = jnp.where(mode % 2 == 0, mode // 2, mode_count - 1 - mode // 2)
        receivers, excitations, weights, position = lax.optimization_barrier(
            (receivers, excitations, weights, position)
        )
        receiver_block = gather_blocks(receivers, "evt", sizes["evt"], 1)
        width = excitations.shape[1] // 2
        first_source = gather_blocks(excitations[:, :width], "sta", sizes["sta"], 0)
        row_count, block_modes = receiver_block.shape
        chunk = row_count // mode_count
        half = chunk // 2

        def partial_rows(owner, part, source_block, receiver_block=receiver_block):
            start = owner * chunk + part * half
            rows = lax.dynamic_slice_in_dim(receiver_block, start, half, axis=0)
            widened = rows.astype(jnp.float32)
            weighted = (widened[:, None, None, :] * weights[None]).astype(jnp.bfloat16)
            product = jnp.dot(
                weighted.reshape(-1, block_modes), source_block, preferred_element_type=jnp.float32
            )
            return product.reshape(half, 2, sample_freqs.shape[0], source_block.shape[1])

        def owner_at(offset):
            place = (position + offset) % mode_count
            if mode_count % 2:
                return place
            return jnp.where(place < mode_count // 2, 2 * place, 2 * (mode_count - 1 - place) + 1)

        def start(source, held=receiver_block):
            return (
                partial_rows(owner_at(-1), 0, source, held),
                partial_rows(owner_at(1), 1, source, held),
            )

        def send(sums):
            return (
                lax.ppermute(sums[0], "mode", clockwise),
                lax.ppermute(sums[1], "mode", counter),
            )

        def add(step, sums, source, held):
            return (
                sums[0] + partial_rows(owner_at(-step - 2), 0, source, held),
                sums[1] + partial_rows(owner_at(step + 2), 1, source, held),
            )

        steps = mode_count - 1
        second_local, _ = lax.optimization_barrier((excitations[:, width:], first_source))
        if sizes["sta"] == 2:
            second_far = swap_pair(second_local, "sta")
        else:
            second_far = lax.all_gather(second_local, "sta", axis=0, tiled=True)
        held, gated, ahead, behind = lax.optimization_barrier(
            (receiver_block, first_source, *start(first_source))
        )
        first = add(0, send((ahead, behind)), gated, held)
        held, second_far, _, _ = lax.optimization_barrier(
            (receiver_block, second_far, first[0], first[1])
        )
        if sizes["sta"] == 2:
            index = lax.axis_index("sta")
            second_source = jnp.concatenate(
                [
                    jnp.where(index == 0, second_local, second_far),
                    jnp.where(index == 0, second_far, second_local),
                ],
                axis=0,
            )
        else:
            second_source = second_far
        second = start(second_source, held)
        for step in range(1, steps):
            held, gated, later, a1, b1, a2, b2 = lax.optimization_barrier(
                (receiver_block, first_source, second_source, *first, *second)
            )
            ahead, behind = send(
                (jnp.concatenate([a1, a2], axis=3), jnp.concatenate([b1, b2], axis=3))
            )
            first = add(step, (ahead[..., :width], behind[..., :width]), gated, held)
            second = add(step - 1, (ahead[..., width:], behind[..., width:]), later, held)
        held, later, a2, b2 = lax.optimization_barrier(
            (receiver_block, second_source, *second)
        )
        second = add(steps - 1, send((a2, b2)), later, held)
        rows = [jnp.concatenate(parts, axis=3) for parts in zip(first, second)]
        return jnp.concatenate(rows, axis=0)

    return per_device


def solution(mesh):
    placed = (P("sta", ("mode", "evt")), P(("mode", "sta"), "evt"), P("mode"), P("mode"), P())
    return jax.shard_map(
        make_per_device(dict(mesh.shape)),
        mesh=mesh,
        in_specs=placed,
        out_specs=P(("sta", "mode"), None, None, "evt"),
        check_vma=False,
    )
```

```python
import jax
import jax.numpy as jnp
from jax import lax
from jax.sharding import PartitionSpec as P


def resonance(mode_freqs, mode_damping, frequency):
    offset = mode_freqs - frequency
    denominator = offset * offset + mode_damping * mode_damping
    return (mode_damping / denominator, -offset / denominator)


def ring_order(count):
    if count % 2:
        return list(range(count))
    return [2 * i for i in range(count // 2)] + [2 * i + 1 for i in reversed(range(count // 2))]


def swap_pair(local, axis_name):
    return lax.ppermute(local, axis_name, [(0, 1), (1, 0)])


def gather_blocks(local, axis_name, size, axis):
    if size != 2:
        return lax.all_gather(local, axis_name, axis=axis, tiled=True)
    other = swap_pair(local, axis_name)
    index = lax.axis_index(axis_name)
    first = jnp.where(index == 0, local, other)
    second = jnp.where(index == 0, other, local)
    return jnp.concatenate([first, second], axis=axis)


def make_per_device(sizes):
    mode_count = sizes["mode"]
    order = ring_order(mode_count)
    position_of = [0] * mode_count
    for position, device in enumerate(order):
        position_of[device] = position
    clockwise = [(order[i], order[(i + 1) % mode_count]) for i in range(mode_count)]
    counter = [(order[(i + 1) % mode_count], order[i]) for i in range(mode_count)]

    def per_device(receivers, excitations, mode_freqs, mode_damping, sample_freqs):
        mode = lax.axis_index("mode")
        real_weight, imag_weight = resonance(
            mode_freqs[None, :], mode_damping[None, :], sample_freqs[:, None]
        )
        weights = jnp.stack([real_weight, imag_weight], axis=0)
        if mode_count % 2:
            position = mode
        else:
            position = jnp.where(mode % 2 == 0, mode // 2, mode_count - 1 - mode // 2)
        receivers, excitations, weights, position = lax.optimization_barrier(
            (receivers, excitations, weights, position)
        )
        receiver_block = gather_blocks(receivers, "evt", sizes["evt"], 1)
        source_block = gather_blocks(excitations, "sta", sizes["sta"], 0)
        row_count, block_modes = receiver_block.shape
        chunk = row_count // mode_count
        half = chunk // 4

        def partial_rows(owner, part, receiver_block=receiver_block):
            start = owner * chunk + part * half
            rows = lax.dynamic_slice_in_dim(receiver_block, start, half, axis=0)
            widened = rows.astype(jnp.float32)
            weighted = (widened[:, None, None, :] * weights[None]).astype(jnp.bfloat16)
            product = jnp.dot(
                weighted.reshape(-1, block_modes), source_block, preferred_element_type=jnp.float32
            )
            return product.reshape(half, 2, sample_freqs.shape[0], source_block.shape[1])

        def owner_at(offset):
            place = (position + offset) % mode_count
            if mode_count % 2:
                return place
            return jnp.where(place < mode_count // 2, 2 * place, 2 * (mode_count - 1 - place) + 1)

        ahead = [partial_rows(owner_at(-1), part) for part in (0, 1)]
        behind = [partial_rows(owner_at(1), part) for part in (2, 3)]
        for step in range(mode_count - 1):
            for i in range(2):
                held, sent_ahead, sent_behind = lax.optimization_barrier(
                    (receiver_block, ahead[i], behind[i])
                )
                ahead[i] = lax.ppermute(sent_ahead, "mode", clockwise)
                behind[i] = lax.ppermute(sent_behind, "mode", counter)
                ahead[i] = ahead[i] + partial_rows(owner_at(-step - 2), i, held)
                behind[i] = behind[i] + partial_rows(owner_at(step + 2), 2 + i, held)
        return jnp.concatenate(ahead + behind, axis=0)

    return per_device


def solution(mesh):
    placed = (P("sta", ("mode", "evt")), P(("mode", "sta"), "evt"), P("mode"), P("mode"), P())
    return jax.shard_map(
        make_per_device(dict(mesh.shape)),
        mesh=mesh,
        in_specs=placed,
        out_specs=P(("sta", "mode"), None, None, "evt"),
        check_vma=False,
    )
```

```python
import jax
import jax.numpy as jnp
from jax import lax
from jax.sharding import PartitionSpec as P


def resonance(mode_freqs, mode_damping, frequency):
    offset = mode_freqs - frequency
    denominator = offset * offset + mode_damping * mode_damping
    return (mode_damping / denominator, -offset / denominator)


def ring_order(count):
    if count % 2:
        return list(range(count))
    return [2 * i for i in range(count // 2)] + [2 * i + 1 for i in reversed(range(count // 2))]


def swap_pair(local, axis_name):
    return lax.ppermute(local, axis_name, [(0, 1), (1, 0)])


def gather_blocks(local, axis_name, size, axis):
    if size != 2:
        return lax.all_gather(local, axis_name, axis=axis, tiled=True)
    other = swap_pair(local, axis_name)
    index = lax.axis_index(axis_name)
    first = jnp.where(index == 0, local, other)
    second = jnp.where(index == 0, other, local)
    return jnp.concatenate([first, second], axis=axis)


def make_per_device(sizes):
    mode_count = sizes["mode"]
    order = ring_order(mode_count)
    position_of = [0] * mode_count
    for position, device in enumerate(order):
        position_of[device] = position
    clockwise = [(order[i], order[(i + 1) % mode_count]) for i in range(mode_count)]
    counter = [(order[(i + 1) % mode_count], order[i]) for i in range(mode_count)]

    def per_device(receivers, excitations, mode_freqs, mode_damping, sample_freqs):
        mode = lax.axis_index("mode")
        real_weight, imag_weight = resonance(
            mode_freqs[None, :], mode_damping[None, :], sample_freqs[:, None]
        )
        weights = jnp.stack([real_weight, imag_weight], axis=0)
        if mode_count % 2:
            position = mode
        else:
            position = jnp.where(mode % 2 == 0, mode // 2, mode_count - 1 - mode // 2)
        receivers, excitations, weights, position = lax.optimization_barrier(
            (receivers, excitations, weights, position)
        )
        if sizes["sta"] == 2 and sizes["evt"] == 2:
            sta = lax.axis_index("sta")
            same = sta == lax.axis_index("evt")
            other_receivers = swap_pair(receivers, "evt")
            block_modes = receivers.shape[1]
            pieces = [
                (
                    jnp.where(same, receivers, other_receivers),
                    lax.dynamic_slice_in_dim(weights, sta * block_modes, block_modes, axis=2),
                    excitations,
                ),
                (
                    jnp.where(same, other_receivers, receivers),
                    lax.dynamic_slice_in_dim(weights, (1 - sta) * block_modes, block_modes, axis=2),
                    swap_pair(excitations, "sta"),
                ),
            ]
        else:
            pieces = [
                (
                    gather_blocks(receivers, "evt", sizes["evt"], 1),
                    weights,
                    gather_blocks(excitations, "sta", sizes["sta"], 0),
                )
            ]
        row_count = receivers.shape[0]
        events = excitations.shape[1]
        chunk = row_count // mode_count
        half = chunk // 2

        def partial_rows(owner, part, held=pieces):
            start = owner * chunk + part * half
            total = None
            for receiver_block, piece_weights, source_block in held:
                rows = lax.dynamic_slice_in_dim(receiver_block, start, half, axis=0)
                widened = rows.astype(jnp.float32)
                weighted = (widened[:, None, None, :] * piece_weights[None]).astype(jnp.bfloat16)
                product = jnp.dot(
                    weighted.reshape(-1, receiver_block.shape[1]),
                    source_block,
                    preferred_element_type=jnp.float32,
                )
                total = product if total is None else total + product
            return total.reshape(half, 2, sample_freqs.shape[0], events)

        def owner_at(offset):
            place = (position + offset) % mode_count
            if mode_count % 2:
                return place
            return jnp.where(place < mode_count // 2, 2 * place, 2 * (mode_count - 1 - place) + 1)

        ahead = partial_rows(owner_at(-1), 0)
        behind = partial_rows(owner_at(1), 1)
        for step in range(mode_count - 1):
            held, ahead, behind = lax.optimization_barrier((pieces, ahead, behind))
            ahead = lax.ppermute(ahead, "mode", clockwise)
            behind = lax.ppermute(behind, "mode", counter)
            ahead = ahead + partial_rows(owner_at(-step - 2), 0, held)
            behind = behind + partial_rows(owner_at(step + 2), 1, held)
        return jnp.concatenate([ahead, behind], axis=0)

    return per_device


def solution(mesh):
    placed = (P("sta", ("mode", "evt")), P(("mode", "sta"), "evt"), P("mode"), P("mode"), P())
    return jax.shard_map(
        make_per_device(dict(mesh.shape)),
        mesh=mesh,
        in_specs=placed,
        out_specs=P(("sta", "mode"), None, None, "evt"),
        check_vma=False,
    )
```

```python
import jax
import jax.numpy as jnp
from jax import lax
from jax.sharding import PartitionSpec as P


def resonance(mode_freqs, mode_damping, frequency):
    offset = mode_freqs - frequency
    denominator = offset * offset + mode_damping * mode_damping
    return (mode_damping / denominator, -offset / denominator)


def ring_order(count):
    if count % 2:
        return list(range(count))
    return [2 * i for i in range(count // 2)] + [2 * i + 1 for i in reversed(range(count // 2))]


def swap_pair(local, axis_name):
    return lax.ppermute(local, axis_name, [(0, 1), (1, 0)])


def gather_blocks(local, axis_name, size, axis):
    if size != 2:
        return lax.all_gather(local, axis_name, axis=axis, tiled=True)
    other = swap_pair(local, axis_name)
    index = lax.axis_index(axis_name)
    first = jnp.where(index == 0, local, other)
    second = jnp.where(index == 0, other, local)
    return jnp.concatenate([first, second], axis=axis)


def make_per_device(sizes):
    mode_count = sizes["mode"]
    order = ring_order(mode_count)
    position_of = [0] * mode_count
    for position, device in enumerate(order):
        position_of[device] = position
    clockwise = [(order[i], order[(i + 1) % mode_count]) for i in range(mode_count)]
    counter = [(order[(i + 1) % mode_count], order[i]) for i in range(mode_count)]

    def per_device(receivers, excitations, mode_freqs, mode_damping, sample_freqs):
        mode = lax.axis_index("mode")
        real_weight, imag_weight = resonance(
            mode_freqs[None, :], mode_damping[None, :], sample_freqs[:, None]
        )
        weights = jnp.stack([real_weight, imag_weight], axis=0)
        if mode_count % 2:
            position = mode
        else:
            position = jnp.where(mode % 2 == 0, mode // 2, mode_count - 1 - mode // 2)
        receivers, excitations, weights, position = lax.optimization_barrier(
            (receivers, excitations, weights, position)
        )
        row_count = receivers.shape[0]
        chunk = row_count // mode_count
        half = chunk // 2

        def owner_at(offset):
            place = (position + offset) % mode_count
            if mode_count % 2:
                return place
            return jnp.where(place < mode_count // 2, 2 * place, 2 * (mode_count - 1 - place) + 1)

        first_rows = jnp.concatenate(
            [
                lax.dynamic_slice_in_dim(receivers, owner_at(-1) * chunk, half, axis=0),
                lax.dynamic_slice_in_dim(receivers, owner_at(1) * chunk + half, half, axis=0),
            ],
            axis=0,
        )
        first_block = gather_blocks(first_rows, "evt", sizes["evt"], 1)
        source_block = gather_blocks(excitations, "sta", sizes["sta"], 0)
        later_receivers, source_block = lax.optimization_barrier((receivers, source_block))
        receiver_block = gather_blocks(later_receivers, "evt", sizes["evt"], 1)
        block_modes = receiver_block.shape[1]

        def weighted_product(rows):
            widened = rows.astype(jnp.float32)
            weighted = (widened[:, None, None, :] * weights[None]).astype(jnp.bfloat16)
            product = jnp.dot(
                weighted.reshape(-1, block_modes), source_block, preferred_element_type=jnp.float32
            )
            return product.reshape(half, 2, sample_freqs.shape[0], source_block.shape[1])

        def partial_rows(owner, part):
            start = owner * chunk + part * half
            return weighted_product(lax.dynamic_slice_in_dim(receiver_block, start, half, axis=0))

        ahead = weighted_product(first_block[:half])
        behind = weighted_product(first_block[half:])
        for step in range(mode_count - 1):
            ahead = lax.ppermute(ahead, "mode", clockwise)
            behind = lax.ppermute(behind, "mode", counter)
            ahead = ahead + partial_rows(owner_at(-step - 2), 0)
            behind = behind + partial_rows(owner_at(step + 2), 1)
        return jnp.concatenate([ahead, behind], axis=0)

    return per_device


def solution(mesh):
    placed = (P("sta", ("mode", "evt")), P(("mode", "sta"), "evt"), P("mode"), P("mode"), P())
    return jax.shard_map(
        make_per_device(dict(mesh.shape)),
        mesh=mesh,
        in_specs=placed,
        out_specs=P(("sta", "mode"), None, None, "evt"),
        check_vma=False,
    )
```
